128 devices in a mesh: section: 16 (over y, z_lo, core), sp: 8 (over z_hi, x).
Axes of the slice: x: 4, y: 4, z: 4 (z_hi: 2, z_lo: 2; z = z_hi * 2 + z_lo), core: 2. Of those that a mesh axis runs over, the one named last changes fastest.
Arguments:
- resid: float32 [16, 896, 6144], P('section', 'sp'), may hold values from -1.8 to 1.8
- qkv: bfloat16 [16, 896, 3, 6144], P('section', 'sp'), may hold values from -48 to 48
- cache_kv: bfloat16 [16, 2, 2, 1344, 6144], P('section', None, None, None, 'sp'), may hold values from -6 to 6
- out_proj: bfloat16 [16, 6144, 6144], P('section', 'sp'), may hold values from -0.078125 to 0.078125
- gate: float32 [16, 2, 6144], P('section'), may hold values from 0.5 to 2
- span_ids: int32 [16], P('section'), may hold values from 3 to 39
- cache_counts: int32 [16], P('section'), may hold values from 0 to 3, as said below
- span_mask: int32 [40, 40], replicated, may hold values from 0 to 1, as said below
Outputs:
- carried: float32 [16, 896, 6144], P('section', 'sp')
The draws below stay inside these ranges and needn't reach their ends.
Inputs may be any that keep to these rules, and one draw needn't show every extreme that they name: `cache_counts`: some section has all 3 slots filled. span_mask[i][j] is 0 for j > i and 1 for j = i.
All inputs are finite; a program needn't handle non-finite values.
Results may differ from the reference program's by a relative error of at most 0.006.
Values may be sent and summed in bfloat16 or wider, within the bound.
No kernel may reach another device: no remote copies, remote signals or barrier semaphores. Data moves between devices by JAX's collectives and lax.ppermute only.
A program may use at most 384 MiB of HBM per device.

```python
import jax
import jax.numpy as jnp
from jax import lax

D = 6144
HEADS = 48
HDIM = 128
SPAN = 448
NCHUNK = 40
SLOTS = 3
VIDS = 2
SECTIONS = 16
TOKS = 896
HD = 6144
KEYS = 1344


def draw_qkv(key, part):
    key_base = jax.random.fold_in(key, 0)
    shape = (SECTIONS, TOKS, 3, HD)
    channel = jnp.array([2.0, 1.0, 1.0], jnp.float32)[None, None, :, None]
    result = jnp.clip(jax.random.normal(key_base, shape, jnp.float32), -6.0, 6.0) * channel
    return result.astype(jnp.bfloat16)


def draw_cache_counts(key, part):
    key_fill, key_full = jax.random.split(key)
    filled = jax.random.randint(key_fill, (SECTIONS,), 0, SLOTS + 1, dtype=jnp.int32)
    fullest = jax.random.randint(key_full, (), 0, SECTIONS, dtype=jnp.int32)
    return jnp.where(jnp.arange(SECTIONS, dtype=jnp.int32) == fullest, SLOTS, filled).astype(jnp.int32)


def draw_span_mask(key, part):
    coins = jax.random.randint(key, (NCHUNK, NCHUNK), 0, 4, dtype=jnp.int32)
    row_index = jnp.arange(NCHUNK, dtype=jnp.int32)[:, None]
    col_index = jnp.arange(NCHUNK, dtype=jnp.int32)[None, :]
    earlier = jnp.where(coins > 0, 1, 0)
    return jnp.where(col_index < row_index, earlier, jnp.where(col_index == row_index, 1, 0)).astype(jnp.int32)


def with_ends(values, own_key, low, high):
    extent = values.shape
    place = [jax.random.randint(jax.random.fold_in(own_key, axis), (), 0, extent[axis]) for axis in range(len(extent))]
    values = values.at[tuple(place)].set(low)
    longest = extent.index(max(extent))
    place[longest] = (place[longest] + 1) % extent[longest]
    return values.at[tuple(place)].set(high)


def level_of(stream_key, extent, shards, low, top_value):
    def one(axis_at, blocks):
        heights = jax.random.uniform(jax.random.fold_in(jax.random.fold_in(stream_key, 6), axis_at), (blocks,), jnp.float32, low / len(shards), top_value / len(shards))
        return jnp.repeat(jnp.exp(heights), extent[axis_at] // blocks).reshape((-1,) + (1,) * (len(extent) - axis_at - 1))

    factor_of = one(*shards[0])
    for cut in shards[1:]:
        factor_of = factor_of * one(*cut)
    return factor_of


def centred(rng, extent, width, limit, shards=(), kind=jnp.bfloat16):
    factor_of = level_of(rng, extent, shards, -0.22, 0.18) if shards else 1.0
    values = jax.random.normal(rng, extent, jnp.float32) * width * factor_of
    return jnp.minimum(jnp.maximum(values, -limit), limit).astype(kind)


def setup_inputs(seed: int = 0) -> dict:
    splits = jax.random.split(jax.random.key(seed), 9)
    resid = centred(splits[0], (SECTIONS, TOKS, D), 0.3, 1.8, ((0, 16), (1, 8)), jnp.float32)
    qkv = draw_qkv(jax.random.fold_in(splits[8], 71), 0)
    cache_kv = centred(splits[2], (SECTIONS, 2, VIDS, KEYS, HD), 1.0, 6.0, ((0, 16), (4, 8)))
    out_proj = centred(splits[3], (SECTIONS, HD, D), HD ** -0.5, 0.078125, ((0, 16), (1, 8)))
    gate = jnp.clip(0.5 + 1.5 * jax.random.uniform(splits[4], (SECTIONS, VIDS, D), jnp.float32) ** level_of(splits[4], (SECTIONS, VIDS, D), ((0, 16),), -0.2, 0.2), 0.5, 2.0)
    span_ids = with_ends(jax.random.randint(splits[5], (SECTIONS,), SLOTS, NCHUNK), jax.random.fold_in(splits[5], 1), SLOTS, NCHUNK - 1).astype(jnp.int32)
    cache_counts = draw_cache_counts(jax.random.fold_in(splits[8], 71), 0)
    span_mask = draw_span_mask(jax.random.fold_in(splits[8], 71), 0)
    return {"resid": resid, "qkv": qkv, "cache_kv": cache_kv, "out_proj": out_proj, "gate": gate, "span_ids": span_ids, "cache_counts": cache_counts, "span_mask": span_mask}


def visible_slots(span_id, filled, span_mask):
    row_mask = lax.dynamic_index_in_dim(span_mask, span_id, 0, keepdims=False)
    slot_ids = jnp.arange(SLOTS, dtype=jnp.int32)
    wanted = span_id - 1 - slot_ids
    columns = jnp.arange(NCHUNK, dtype=jnp.int32)
    looked = jnp.sum(jnp.where(columns[None, :] == wanted[:, None], row_mask[None, :], 0), axis=1)
    return (slot_ids < filled) & (looked == 1)


def attend(queries, own_keys, own_values, cache_keys, cache_values, key_live):
    score_scale = HDIM ** -0.5
    keys_all = jnp.concatenate([cache_keys, own_keys], axis=0).astype(jnp.float32)
    values_all = jnp.concatenate([cache_values, own_values], axis=0).astype(jnp.float32)
    scores = jnp.einsum("qhe,khe->hqk", queries.astype(jnp.float32), keys_all) * score_scale
    live_all = jnp.concatenate([key_live, jnp.ones((SPAN,), dtype=bool)])
    scores = jnp.where(live_all[None, None, :], scores, -jnp.inf)
    highest = jnp.max(scores, axis=2, keepdims=True)
    raised = jnp.exp(scores - highest)
    weights = (raised / jnp.sum(raised, axis=2, keepdims=True)).astype(jnp.bfloat16)
    mixed = jnp.einsum("hqk,khe->qhe", weights.astype(jnp.float32), values_all)
    return mixed.astype(jnp.bfloat16).reshape(SPAN, HD)


def reference(resid, qkv, cache_kv, out_proj, gate, span_ids, cache_counts, span_mask):
    def one_section(inputs_one):
        resid_one, qkv_one, cache_one, proj_one, gate_one, span_id, filled = inputs_one
        live_slots = visible_slots(span_id, filled, span_mask)
        key_live = jnp.repeat(live_slots, SPAN)
        split_rows = qkv_one.reshape(VIDS, SPAN, 3, HEADS, HDIM)
        cache_keys = cache_one[0].reshape(VIDS, KEYS, HEADS, HDIM)
        cache_values = cache_one[1].reshape(VIDS, KEYS, HEADS, HDIM)

        def one_video(video_in):
            return attend(video_in[0], video_in[1], video_in[2], video_in[3], video_in[4], key_live)

        heads_out = lax.map(one_video, (split_rows[:, :, 0], split_rows[:, :, 1], split_rows[:, :, 2], cache_keys, cache_values))
        heads_out = heads_out.reshape(TOKS, HD)
        projected = jnp.dot(heads_out, proj_one, preferred_element_type=jnp.float32)
        video_of = jnp.arange(TOKS, dtype=jnp.int32) // SPAN
        return resid_one + gate_one[video_of] * projected

    layer_out = lax.map(one_section, (resid, qkv, cache_kv, out_proj, gate, span_ids, cache_counts))
    return jnp.roll(layer_out, 1, axis=0)
```

```python
import jax
import jax.numpy as jnp
from jax import lax
from jax.sharding import PartitionSpec as P

HDIM = 128
SPAN = 448
NCHUNK = 40
SLOTS = 3
VIDS = 2
TOKS = 896
KEYS = 1344


def passed_along(shard, axis, by):
    devices = lax.axis_size(axis)
    return lax.ppermute(shard, axis, [(i, (i + by) % devices) for i in range(devices)])


def visible_slots(span_id, filled, span_mask):
    row_mask = lax.dynamic_index_in_dim(span_mask, span_id, 0, keepdims=False)
    slot_ids = jnp.arange(SLOTS, dtype=jnp.int32)
    wanted = span_id - 1 - slot_ids
    columns = jnp.arange(NCHUNK, dtype=jnp.int32)
    looked = jnp.sum(jnp.where(columns[None, :] == wanted[:, None], row_mask[None, :], 0), axis=1)
    return (slot_ids < filled) & (looked == 1)


def far_scores(queries, cache_keys, live_slots):
    score_scale = HDIM ** (-0.5)
    scores = (
        jnp.einsum("qhe,khe->hqk", queries, cache_keys, preferred_element_type=jnp.float32)
        * score_scale
    )
    key_live = jnp.repeat(live_slots, SPAN)
    result = jnp.where(key_live[None, None, :], scores, -jnp.inf)
    return result


def mix_video(far_part, queries, own_keys, own_values, cache_values):
    score_scale = HDIM ** (-0.5)
    near_part = (
        jnp.einsum("qhe,khe->hqk", queries, own_keys, preferred_element_type=jnp.float32)
        * score_scale
    )
    scores = jnp.concatenate([far_part, near_part], axis=2)
    highest = jnp.max(scores, axis=2, keepdims=True)
    raised = jnp.exp(scores - highest)
    weights = (raised / jnp.sum(raised, axis=2, keepdims=True)).astype(jnp.bfloat16)
    values_all = jnp.concatenate([cache_values, own_values], axis=0)
    mixed = jnp.einsum("hqk,khe->qhe", weights, values_all, preferred_element_type=jnp.float32)
    return mixed.astype(jnp.bfloat16).reshape(SPAN, queries.shape[1] * HDIM)


def per_device(resid, qkv, cache_kv, out_proj, gate, span_ids, cache_counts, span_mask):
    own_rows = resid.shape[1]
    local_width = cache_kv.shape[4]
    local_heads = local_width // HDIM
    filled = cache_counts[0]
    live_slots = visible_slots(span_ids[0], filled, span_mask)
    cache_keys = cache_kv[0, 0].reshape(VIDS, KEYS, local_heads, HDIM)
    cache_values = cache_kv[0, 1].reshape(VIDS, KEYS, local_heads, HDIM)

    def score_video(inputs_one):
        return far_scores(inputs_one[0], inputs_one[1], live_slots)

    spread = lax.all_to_all(qkv[0], "sp", split_axis=2, concat_axis=0, tiled=True)
    queries = spread[:, 0].reshape(VIDS, SPAN, local_heads, HDIM)
    far_all = lax.map(score_video, (queries, cache_keys))
    own_keys = spread[:, 1].reshape(VIDS, SPAN, local_heads, HDIM)
    own_values = spread[:, 2].reshape(VIDS, SPAN, local_heads, HDIM)

    def mix_one(inputs_one):
        return mix_video(inputs_one[0], inputs_one[1], inputs_one[2], inputs_one[3], inputs_one[4])

    heads_all = lax.map(mix_one, (far_all, queries, own_keys, own_values, cache_values)).reshape(
        TOKS, local_width
    )
    partial = jnp.dot(heads_all, out_proj[0], preferred_element_type=jnp.float32)
    devices = lax.axis_size("sp")
    shares = partial.astype(jnp.bfloat16).reshape(devices, own_rows, partial.shape[1])
    shares = lax.all_to_all(shares, "sp", 0, 0, tiled=True)
    projected = jnp.sum(shares.astype(jnp.float32), axis=0)
    device_place = lax.axis_index("sp")
    video_of = (device_place * own_rows + jnp.arange(own_rows, dtype=jnp.int32)) // SPAN
    picker = (video_of[:, None] == jnp.arange(VIDS, dtype=jnp.int32)[None, :]).astype(jnp.float32)
    gains = jnp.dot(picker, gate[0], precision=lax.Precision.HIGHEST)
    layer_out = resid[0] + gains * projected
    return passed_along(layer_out[None], "section", 1)


def solution(mesh):
    in_specs = (
        P("section", "sp", None),
        P("section", "sp", None, None),
        P("section", None, None, None, "sp"),
        P("section", "sp", None),
        P("section", None, None),
        P("section"),
        P("section"),
        P(),
    )
    out_specs = P("section", "sp", None)
    return jax.shard_map(
        per_device, mesh=mesh, in_specs=in_specs, out_specs=out_specs, check_vma=False
    )
```

```python
import jax
import jax.numpy as jnp
from jax import lax
from jax.experimental import pallas as pl
from jax.experimental.pallas import tpu as pltpu
from jax.sharding import PartitionSpec as P

HDIM = 128
SPAN = 448
NCHUNK = 40
SLOTS = 3
VIDS = 2
TOKS = 896
KEYS = 1344


def passed_along(shard, axis, by):
    devices = lax.axis_size(axis)
    return lax.ppermute(shard, axis, [(i, (i + by) % devices) for i in range(devices)])


def visible_slots(span_id, filled, span_mask):
    row_mask = lax.dynamic_index_in_dim(span_mask, span_id, 0, keepdims=False)
    slot_ids = jnp.arange(SLOTS, dtype=jnp.int32)
    wanted = span_id - 1 - slot_ids
    columns = jnp.arange(NCHUNK, dtype=jnp.int32)
    looked = jnp.sum(jnp.where(columns[None, :] == wanted[:, None], row_mask[None, :], 0), axis=1)
    return (slot_ids < filled) & (looked == 1)


def attend_kernel(bias_ref, q_ref, kn_ref, vn_ref, kc_ref, vc_ref, out_ref):
    score_scale = HDIM ** (-0.5)
    q = q_ref[...].reshape(SPAN, HDIM)
    kn = kn_ref[...].reshape(SPAN, HDIM)
    vn = vn_ref[...].reshape(SPAN, HDIM)
    kc = kc_ref[0, 0]
    vc = vc_ref[0, 0]
    contract = (((1,), (1,)), ((), ()))
    far = lax.dot_general(q, kc, contract, preferred_element_type=jnp.float32) * score_scale
    far = far + bias_ref[...]
    near = lax.dot_general(q, kn, contract, preferred_element_type=jnp.float32) * score_scale
    highest = jnp.maximum(jnp.max(far, axis=1, keepdims=True), jnp.max(near, axis=1, keepdims=True))
    far_raised = jnp.exp(far - highest)
    near_raised = jnp.exp(near - highest)
    total = jnp.sum(far_raised, axis=1, keepdims=True) + jnp.sum(near_raised, axis=1, keepdims=True)
    far_w = (far_raised / total).astype(jnp.bfloat16)
    near_w = (near_raised / total).astype(jnp.bfloat16)
    mixed = jnp.dot(far_w, vc, preferred_element_type=jnp.float32) + jnp.dot(
        near_w, vn, preferred_element_type=jnp.float32
    )
    out_ref[...] = mixed.astype(out_ref.dtype)


def attend_all(key_bias, spread, cache_kv, local_heads):
    groups = spread.shape[0]
    per_video = groups // VIDS
    rows = spread.shape[1]
    width = local_heads * HDIM

    def own_spec(part):
        return pl.BlockSpec((per_video, rows, HDIM), lambda b, h: (b, 0, part * local_heads + h))

    return pl.pallas_call(
        attend_kernel,
        grid=(VIDS, local_heads),
        in_specs=[
            pl.BlockSpec((1, KEYS), lambda b, h: (0, 0)),
            own_spec(0),
            own_spec(1),
            own_spec(2),
            pl.BlockSpec((1, 1, KEYS, HDIM), lambda b, h: (0, b, 0, h)),
            pl.BlockSpec((1, 1, KEYS, HDIM), lambda b, h: (1, b, 0, h)),
        ],
        out_specs=pl.BlockSpec((SPAN, HDIM), lambda b, h: (b, h)),
        out_shape=jax.ShapeDtypeStruct((TOKS, width), jnp.bfloat16),
    )(key_bias, spread, spread, spread, cache_kv, cache_kv)


def per_device(resid, qkv, cache_kv, out_proj, gate, span_ids, cache_counts, span_mask):
    own_rows = resid.shape[1]
    local_width = cache_kv.shape[4]
    local_heads = local_width // HDIM
    devices = lax.axis_size("sp")
    filled = cache_counts[0]
    live_slots = visible_slots(span_ids[0], filled, span_mask)
    key_bias = jnp.repeat(jnp.where(live_slots, 0.0, -jnp.inf).astype(jnp.float32), SPAN)[None, :]

    grouped = qkv[0].reshape(own_rows, 3, devices, local_width).transpose(2, 0, 1, 3)
    spread = lax.all_to_all(grouped, "sp", 0, 0, tiled=True)
    spread = spread.reshape(devices, own_rows, 3 * local_width)
    heads_all = attend_all(key_bias, spread, cache_kv[0], local_heads)

    partial = jnp.dot(heads_all, out_proj[0], preferred_element_type=jnp.float32)
    shares = partial.astype(jnp.bfloat16).reshape(devices, own_rows, partial.shape[1])
    shares = lax.all_to_all(shares, "sp", 0, 0, tiled=True)
    projected = jnp.sum(shares.astype(jnp.float32), axis=0)
    device_place = lax.axis_index("sp")
    video_of = (device_place * own_rows + jnp.arange(own_rows, dtype=jnp.int32)) // SPAN
    picker = (video_of[:, None] == jnp.arange(VIDS, dtype=jnp.int32)[None, :]).astype(jnp.float32)
    gains = jnp.dot(picker, gate[0], precision=lax.Precision.HIGHEST)
    layer_out = resid[0] + gains * projected
    return passed_along(layer_out[None], "section", 1)


def solution(mesh):
    in_specs = (
        P("section", "sp", None),
        P("section", "sp", None, None),
        P("section", None, None, None, "sp"),
        P("section", "sp", None),
        P("section", None, None),
        P("section"),
        P("section"),
        P(),
    )
    out_specs = P("section", "sp", None)
    return jax.shard_map(
        per_device, mesh=mesh, in_specs=in_specs, out_specs=out_specs, check_vma=False
    )
```

```python
import jax
import jax.numpy as jnp
from jax import lax
from jax.experimental import pallas as pl
from jax.experimental.pallas import tpu as pltpu
from jax.sharding import PartitionSpec as P

HDIM = 128
SPAN = 448
NCHUNK = 40
SLOTS = 3
VIDS = 2
TOKS = 896
KEYS = 1344


def passed_along(shard, axis, by):
    devices = lax.axis_size(axis)
    return lax.ppermute(shard, axis, [(i, (i + by) % devices) for i in range(devices)])


def visible_slots(span_id, filled, span_mask):
    row_mask = lax.dynamic_index_in_dim(span_mask, span_id, 0, keepdims=False)
    slot_ids = jnp.arange(SLOTS, dtype=jnp.int32)
    wanted = span_id - 1 - slot_ids
    columns = jnp.arange(NCHUNK, dtype=jnp.int32)
    looked = jnp.sum(jnp.where(columns[None, :] == wanted[:, None], row_mask[None, :], 0), axis=1)
    return (slot_ids < filled) & (looked == 1)


def attend_kernel(bias_ref, q_ref, kn_ref, vn_ref, kc_ref, vc_ref, out_ref):
    score_scale = HDIM ** (-0.5)
    q = q_ref[...].reshape(SPAN, HDIM)
    kn = kn_ref[...].reshape(SPAN, HDIM)
    vn = vn_ref[...].reshape(SPAN, HDIM)
    kc = kc_ref[0, 0]
    vc = vc_ref[0, 0]
    contract = (((1,), (1,)), ((), ()))
    far = lax.dot_general(q, kc, contract, preferred_element_type=jnp.float32) * score_scale
    far = far + bias_ref[...]
    near = lax.dot_general(q, kn, contract, preferred_element_type=jnp.float32) * score_scale
    highest = jnp.maximum(jnp.max(far, axis=1, keepdims=True), jnp.max(near, axis=1, keepdims=True))
    far_raised = jnp.exp(far - highest)
    near_raised = jnp.exp(near - highest)
    total = jnp.sum(far_raised, axis=1, keepdims=True) + jnp.sum(near_raised, axis=1, keepdims=True)
    far_w = (far_raised / total).astype(jnp.bfloat16)
    near_w = (near_raised / total).astype(jnp.bfloat16)
    mixed = jnp.dot(far_w, vc, preferred_element_type=jnp.float32) + jnp.dot(
        near_w, vn, preferred_element_type=jnp.float32
    )
    out_ref[...] = mixed.astype(out_ref.dtype)


def attend_all(key_bias, spread, cache_kv, local_heads):
    groups = spread.shape[0]
    per_video = groups // VIDS
    rows = spread.shape[1]
    width = local_heads * HDIM

    def own_spec(part):
        return pl.BlockSpec((per_video, rows, HDIM), lambda b, h: (b, 0, part * local_heads + h))

    return pl.pallas_call(
        attend_kernel,
        grid=(VIDS, local_heads),
        in_specs=[
            pl.BlockSpec((1, KEYS), lambda b, h: (0, 0)),
            own_spec(0),
            own_spec(1),
            own_spec(2),
            pl.BlockSpec((1, 1, KEYS, HDIM), lambda b, h: (0, b, 0, h)),
            pl.BlockSpec((1, 1, KEYS, HDIM), lambda b, h: (1, b, 0, h)),
        ],
        out_specs=pl.BlockSpec((SPAN, HDIM), lambda b, h: (b, h)),
        out_shape=jax.ShapeDtypeStruct((TOKS, width), jnp.bfloat16),
    )(key_bias, spread, spread, spread, cache_kv, cache_kv)


def per_device(resid, qkv, cache_kv, out_proj, gate, span_ids, cache_counts, span_mask):
    own_rows = resid.shape[1]
    local_width = cache_kv.shape[4]
    local_heads = local_width // HDIM
    devices = lax.axis_size("sp")
    filled = cache_counts[0]
    live_slots = visible_slots(span_ids[0], filled, span_mask)
    key_bias = jnp.repeat(jnp.where(live_slots, 0.0, -jnp.inf).astype(jnp.float32), SPAN)[None, :]

    grouped = qkv[0].reshape(own_rows, 3, devices, local_width).transpose(2, 0, 1, 3)
    spread = lax.all_to_all(grouped, "sp", 0, 0, tiled=True)
    spread = spread.reshape(devices, own_rows, 3 * local_width)
    heads_all = attend_all(key_bias, spread, cache_kv[0], local_heads)

    device_place = lax.axis_index("sp")
    video_of = (device_place * own_rows + jnp.arange(own_rows, dtype=jnp.int32)) // SPAN
    picker = (video_of[:, None] == jnp.arange(VIDS, dtype=jnp.int32)[None, :]).astype(jnp.float32)
    gains = jnp.dot(picker, gate[0], precision=lax.Precision.HIGHEST)
    width = out_proj.shape[2]
    pieces = 3
    step = width // pieces
    outs = []
    for c in range(pieces):
        cols = slice(c * step, (c + 1) * step)
        partial = jnp.dot(heads_all, out_proj[0, :, cols], preferred_element_type=jnp.float32)
        shares = partial.astype(jnp.bfloat16).reshape(devices, own_rows, step)
        shares = lax.all_to_all(shares, "sp", 0, 0, tiled=True)
        projected = jnp.sum(shares.astype(jnp.float32), axis=0)
        layer_out = resid[0, :, cols] + gains[:, cols] * projected
        outs.append(passed_along(layer_out, "section", 1))
    return jnp.concatenate(outs, axis=1)[None]


def solution(mesh):
    in_specs = (
        P("section", "sp", None),
        P("section", "sp", None, None),
        P("section", None, None, None, "sp"),
        P("section", "sp", None),
        P("section", None, None),
        P("section"),
        P("section"),
        P(),
    )
    out_specs = P("section", "sp", None)
    return jax.shard_map(
        per_device, mesh=mesh, in_specs=in_specs, out_specs=out_specs, check_vma=False
    )
```

```python
import jax
import jax.numpy as jnp
from jax import lax
from jax.experimental import pallas as pl
from jax.experimental.pallas import tpu as pltpu
from jax.sharding import PartitionSpec as P

HDIM = 128
SPAN = 448
NCHUNK = 40
SLOTS = 3
VIDS = 2
TOKS = 896
KEYS = 1344


def passed_along(shard, axis, by):
    devices = lax.axis_size(axis)
    return lax.ppermute(shard, axis, [(i, (i + by) % devices) for i in range(devices)])


def visible_slots(span_id, filled, span_mask):
    row_mask = lax.dynamic_index_in_dim(span_mask, span_id, 0, keepdims=False)
    slot_ids = jnp.arange(SLOTS, dtype=jnp.int32)
    wanted = span_id - 1 - slot_ids
    columns = jnp.arange(NCHUNK, dtype=jnp.int32)
    looked = jnp.sum(jnp.where(columns[None, :] == wanted[:, None], row_mask[None, :], 0), axis=1)
    return (slot_ids < filled) & (looked == 1)


def attend_kernel(bias_ref, q_ref, kn_ref, vn_ref, kc_ref, vc_ref, out_ref):
    score_scale = HDIM ** (-0.5)
    q = q_ref[...].reshape(SPAN, HDIM)
    kn = kn_ref[...].reshape(SPAN, HDIM)
    vn = vn_ref[...].reshape(SPAN, HDIM)
    kc = kc_ref[0, 0]
    vc = vc_ref[0, 0]
    contract = (((1,), (1,)), ((), ()))
    far = lax.dot_general(q, kc, contract, preferred_element_type=jnp.float32) * score_scale
    far = far + bias_ref[...]
    near = lax.dot_general(q, kn, contract, preferred_element_type=jnp.float32) * score_scale
    highest = jnp.maximum(jnp.max(far, axis=1, keepdims=True), jnp.max(near, axis=1, keepdims=True))
    far_raised = jnp.exp(far - highest)
    near_raised = jnp.exp(near - highest)
    total = jnp.sum(far_raised, axis=1, keepdims=True) + jnp.sum(near_raised, axis=1, keepdims=True)
    far_w = (far_raised / total).astype(jnp.bfloat16)
    near_w = (near_raised / total).astype(jnp.bfloat16)
    mixed = jnp.dot(far_w, vc, preferred_element_type=jnp.float32) + jnp.dot(
        near_w, vn, preferred_element_type=jnp.float32
    )
    out_ref[...] = mixed.astype(out_ref.dtype)


def attend_all(key_bias, spread, cache_kv, local_heads):
    groups = spread.shape[0]
    per_video = groups // VIDS
    rows = spread.shape[1]
    width = local_heads * HDIM

    def own_spec(part):
        return pl.BlockSpec((per_video, rows, HDIM), lambda b, h: (b, 0, part * local_heads + h))

    return pl.pallas_call(
        attend_kernel,
        grid=(VIDS, local_heads),
        in_specs=[
            pl.BlockSpec((1, KEYS), lambda b, h: (0, 0)),
            own_spec(0),
            own_spec(1),
            own_spec(2),
            pl.BlockSpec((1, 1, KEYS, HDIM), lambda b, h: (0, b, 0, h)),
            pl.BlockSpec((1, 1, KEYS, HDIM), lambda b, h: (1, b, 0, h)),
        ],
        out_specs=pl.BlockSpec((SPAN, HDIM), lambda b, h: (b, h)),
        out_shape=jax.ShapeDtypeStruct((TOKS, width), jnp.bfloat16),
    )(key_bias, spread, spread, spread, cache_kv, cache_kv)


def per_device(resid, qkv, cache_kv, out_proj, gate, span_ids, cache_counts, span_mask):
    own_rows = resid.shape[1]
    local_width = cache_kv.shape[4]
    local_heads = local_width // HDIM
    devices = lax.axis_size("sp")
    filled = cache_counts[0]
    live_slots = visible_slots(span_ids[0], filled, span_mask)
    key_bias = jnp.repeat(jnp.where(live_slots, 0.0, -jnp.inf).astype(jnp.float32), SPAN)[None, :]

    grouped = qkv[0].reshape(own_rows, 3, devices, local_width).transpose(2, 0, 1, 3)
    spread = lax.all_to_all(grouped, "sp", 0, 0, tiled=True)
    spread = spread.reshape(devices, own_rows, 3 * local_width)
    resid_prev = passed_along(resid[0], "section", 1)
    gate_prev = passed_along(gate[0], "section", 1)
    resid_prev, gate_prev, spread = lax.optimization_barrier((resid_prev, gate_prev, spread))
    heads_all = attend_all(key_bias, spread, cache_kv[0], local_heads)

    device_place = lax.axis_index("sp")
    video_of = (device_place * own_rows + jnp.arange(own_rows, dtype=jnp.int32)) // SPAN
    picker = (video_of[:, None] == jnp.arange(VIDS, dtype=jnp.int32)[None, :]).astype(jnp.float32)
    gains = jnp.dot(picker, gate_prev, precision=lax.Precision.HIGHEST)
    width = out_proj.shape[2]
    pieces = 3
    step = width // pieces
    outs = []
    for c in range(pieces):
        cols = slice(c * step, (c + 1) * step)
        partial = jnp.dot(heads_all, out_proj[0, :, cols], preferred_element_type=jnp.float32)
        shares = partial.astype(jnp.bfloat16).reshape(devices, own_rows, step)
        shares = lax.all_to_all(shares, "sp", 0, 0, tiled=True)
        projected = jnp.sum(shares.astype(jnp.float32), axis=0)
        projected = lax.reduce_precision(projected, 8, 7).astype(jnp.bfloat16)
        projected_prev = passed_along(projected, "section", 1).astype(jnp.float32)
        outs.append(resid_prev[:, cols] + gains[:, cols] * projected_prev)
    return jnp.concatenate(outs, axis=1)[None]


def solution(mesh):
    in_specs = (
        P("section", "sp", None),
        P("section", "sp", None, None),
        P("section", None, None, None, "sp"),
        P("section", "sp", None),
        P("section", None, None),
        P("section"),
        P("section"),
        P(),
    )
    out_specs = P("section", "sp", None)
    return jax.shard_map(
        per_device, mesh=mesh, in_specs=in_specs, out_specs=out_specs, check_vma=False
    )
```

```python
import jax
import jax.numpy as jnp
from jax import lax
from jax.experimental import pallas as pl
from jax.experimental.pallas import tpu as pltpu
from jax.sharding import PartitionSpec as P

HDIM = 128
SPAN = 448
NCHUNK = 40
SLOTS = 3
VIDS = 2
TOKS = 896
KEYS = 1344


def passed_along(shard, axis, by):
    devices = lax.axis_size(axis)
    return lax.ppermute(shard, axis, [(i, (i + by) % devices) for i in range(devices)])


def visible_slots(span_id, filled, span_mask):
    row_mask = lax.dynamic_index_in_dim(span_mask, span_id, 0, keepdims=False)
    slot_ids = jnp.arange(SLOTS, dtype=jnp.int32)
    wanted = span_id - 1 - slot_ids
    columns = jnp.arange(NCHUNK, dtype=jnp.int32)
    looked = jnp.sum(jnp.where(columns[None, :] == wanted[:, None], row_mask[None, :], 0), axis=1)
    return (slot_ids < filled) & (looked == 1)


def attend_kernel(bias_ref, own_ref, kc_ref, vc_ref, out_ref):
    score_scale = HDIM ** (-0.5)
    local_heads = out_ref.shape[1] // HDIM
    width = local_heads * HDIM
    contract = (((1,), (1,)), ((), ()))
    bias = bias_ref[...]
    for h in range(local_heads):
        cols = slice(h * HDIM, (h + 1) * HDIM)
        q = own_ref[:, :, h * HDIM:(h + 1) * HDIM].reshape(SPAN, HDIM)
        kn = own_ref[:, :, width + h * HDIM:width + (h + 1) * HDIM].reshape(SPAN, HDIM)
        vn = own_ref[:, :, 2 * width + h * HDIM:2 * width + (h + 1) * HDIM].reshape(SPAN, HDIM)
        kc = kc_ref[0, 0, :, cols]
        vc = vc_ref[0, 0, :, cols]
        far = lax.dot_general(q, kc, contract, preferred_element_type=jnp.float32) * score_scale
        far = far + bias
        near = lax.dot_general(q, kn, contract, preferred_element_type=jnp.float32) * score_scale
        highest = jnp.maximum(jnp.max(far, axis=1, keepdims=True), jnp.max(near, axis=1, keepdims=True))
        far_raised = jnp.exp(far - highest)
        near_raised = jnp.exp(near - highest)
        total = jnp.sum(far_raised, axis=1, keepdims=True) + jnp.sum(near_raised, axis=1, keepdims=True)
        far_w = (far_raised / total).astype(jnp.bfloat16)
        near_w = (near_raised / total).astype(jnp.bfloat16)
        mixed = jnp.dot(far_w, vc, preferred_element_type=jnp.float32) + jnp.dot(
            near_w, vn, preferred_element_type=jnp.float32
        )
        out_ref[:, cols] = mixed.astype(out_ref.dtype)


def attend_all(key_bias, spread, cache_kv, local_heads):
    groups = spread.shape[0]
    per_video = groups // VIDS
    rows = spread.shape[1]
    width = local_heads * HDIM

    return pl.pallas_call(
        attend_kernel,
        grid=(VIDS,),
        in_specs=[
            pl.BlockSpec((1, KEYS), lambda b: (0, 0)),
            pl.BlockSpec((per_video, rows, 3 * width), lambda b: (b, 0, 0)),
            pl.BlockSpec((1, 1, KEYS, width), lambda b: (0, b, 0, 0)),
            pl.BlockSpec((1, 1, KEYS, width), lambda b: (1, b, 0, 0)),
        ],
        out_specs=pl.BlockSpec((SPAN, width), lambda b: (b, 0)),
        out_shape=jax.ShapeDtypeStruct((TOKS, width), jnp.bfloat16),
    )(key_bias, spread, cache_kv, cache_kv)


def per_device(resid, qkv, cache_kv, out_proj, gate, span_ids, cache_counts, span_mask):
    own_rows = resid.shape[1]
    local_width = cache_kv.shape[4]
    local_heads = local_width // HDIM
    devices = lax.axis_size("sp")
    filled = cache_counts[0]
    live_slots = visible_slots(span_ids[0], filled, span_mask)
    key_bias = jnp.repeat(jnp.where(live_slots, 0.0, -jnp.inf).astype(jnp.float32), SPAN)[None, :]

    grouped = qkv[0].reshape(own_rows, 3, devices, local_width).transpose(2, 0, 1, 3)
    grouped = grouped.reshape(devices, own_rows, 3 * local_width)
    spread = lax.all_to_all(grouped, "sp", 0, 0, tiled=True)
    heads_all = attend_all(key_bias, spread, cache_kv[0], local_heads)

    device_place = lax.axis_index("sp")
    video_of = (device_place * own_rows + jnp.arange(own_rows, dtype=jnp.int32)) // SPAN
    picker = (video_of[:, None] == jnp.arange(VIDS, dtype=jnp.int32)[None, :]).astype(jnp.float32)
    gains = jnp.dot(picker, gate[0], precision=lax.Precision.HIGHEST)
    width = out_proj.shape[2]
    pieces = 3
    step = width // pieces
    outs = []
    for c in range(pieces):
        cols = slice(c * step, (c + 1) * step)
        partial = jnp.dot(heads_all, out_proj[0, :, cols], preferred_element_type=jnp.float32)
        shares = partial.astype(jnp.bfloat16).reshape(devices, own_rows, step)
        shares = lax.all_to_all(shares, "sp", 0, 0, tiled=True)
        projected = jnp.sum(shares.astype(jnp.float32), axis=0)
        layer_out = resid[0, :, cols] + gains[:, cols] * projected
        outs.append(passed_along(layer_out, "section", 1))
    return jnp.concatenate(outs, axis=1)[None]


def solution(mesh):
    in_specs = (
        P("section", "sp", None),
        P("section", "sp", None, None),
        P("section", None, None, None, "sp"),
        P("section", "sp", None),
        P("section", None, None),
        P("section"),
        P("section"),
        P(),
    )
    out_specs = P("section", "sp", None)
    return jax.shard_map(
        per_device, mesh=mesh, in_specs=in_specs, out_specs=out_specs, check_vma=False
    )
```

```python
import jax
import jax.numpy as jnp
from jax import lax
from jax.experimental import pallas as pl
from jax.experimental.pallas import tpu as pltpu
from jax.sharding import PartitionSpec as P

HDIM = 128
SPAN = 448
NCHUNK = 40
SLOTS = 3
VIDS = 2
TOKS = 896
KEYS = 1344


def passed_along(shard, axis, by):
    devices = lax.axis_size(axis)
    return lax.ppermute(shard, axis, [(i, (i + by) % devices) for i in range(devices)])


def visible_slots(span_id, filled, span_mask):
    row_mask = lax.dynamic_index_in_dim(span_mask, span_id, 0, keepdims=False)
    slot_ids = jnp.arange(SLOTS, dtype=jnp.int32)
    wanted = span_id - 1 - slot_ids
    columns = jnp.arange(NCHUNK, dtype=jnp.int32)
    looked = jnp.sum(jnp.where(columns[None, :] == wanted[:, None], row_mask[None, :], 0), axis=1)
    return (slot_ids < filled) & (looked == 1)


def attend_kernel(bias_ref, own_ref, kc_ref, vc_ref, out_ref):
    score_scale = HDIM ** (-0.5)
    local_heads = out_ref.shape[1] // HDIM
    width = local_heads * HDIM
    contract = (((1,), (1,)), ((), ()))
    bias = bias_ref[...]
    for h in range(local_heads):
        cols = slice(h * HDIM, (h + 1) * HDIM)
        q = own_ref[:, :, h * HDIM:(h + 1) * HDIM].reshape(SPAN, HDIM)
        kn = own_ref[:, :, width + h * HDIM:width + (h + 1) * HDIM].reshape(SPAN, HDIM)
        vn = own_ref[:, :, 2 * width + h * HDIM:2 * width + (h + 1) * HDIM].reshape(SPAN, HDIM)
        kc = kc_ref[0, 0, :, cols]
        vc = vc_ref[0, 0, :, cols]
        far = lax.dot_general(q, kc, contract, preferred_element_type=jnp.float32) * score_scale
        far = far + bias
        near = lax.dot_general(q, kn, contract, preferred_element_type=jnp.float32) * score_scale
        highest = jnp.maximum(jnp.max(far, axis=1, keepdims=True), jnp.max(near, axis=1, keepdims=True))
        far_raised = jnp.exp(far - highest)
        near_raised = jnp.exp(near - highest)
        total = jnp.sum(far_raised, axis=1, keepdims=True) + jnp.sum(near_raised, axis=1, keepdims=True)
        far_w = (far_raised / total).astype(jnp.bfloat16)
        near_w = (near_raised / total).astype(jnp.bfloat16)
        mixed = jnp.dot(far_w, vc, preferred_element_type=jnp.float32) + jnp.dot(
            near_w, vn, preferred_element_type=jnp.float32
        )
        out_ref[:, cols] = mixed.astype(out_ref.dtype)


def attend_all(key_bias, spread, cache_kv, local_heads):
    groups = spread.shape[0]
    per_video = groups // VIDS
    rows = spread.shape[1]
    width = local_heads * HDIM

    return pl.pallas_call(
        attend_kernel,
        grid=(VIDS,),
        in_specs=[
            pl.BlockSpec((1, KEYS), lambda b: (0, 0)),
            pl.BlockSpec((per_video, rows, 3 * width), lambda b: (b, 0, 0)),
            pl.BlockSpec((1, 1, KEYS, width), lambda b: (0, b, 0, 0)),
            pl.BlockSpec((1, 1, KEYS, width), lambda b: (1, b, 0, 0)),
        ],
        out_specs=pl.BlockSpec((SPAN, width), lambda b: (b, 0)),
        out_shape=jax.ShapeDtypeStruct((TOKS, width), jnp.bfloat16),
    )(key_bias, spread, cache_kv, cache_kv)


def per_device(resid, qkv, cache_kv, out_proj, gate, span_ids, cache_counts, span_mask):
    own_rows = resid.shape[1]
    local_width = cache_kv.shape[4]
    local_heads = local_width // HDIM
    devices = lax.axis_size("sp")
    filled = cache_counts[0]
    live_slots = visible_slots(span_ids[0], filled, span_mask)
    key_bias = jnp.repeat(jnp.where(live_slots, 0.0, -jnp.inf).astype(jnp.float32), SPAN)[None, :]

    grouped = qkv[0].reshape(own_rows, 3, devices, local_width).transpose(2, 0, 1, 3)
    grouped = grouped.reshape(devices, own_rows, 3 * local_width)
    spread = lax.all_to_all(grouped, "sp", 0, 0, tiled=True)
    heads_all = attend_all(key_bias, spread, cache_kv[0], local_heads)

    device_place = lax.axis_index("sp")
    video_of = (device_place * own_rows + jnp.arange(own_rows, dtype=jnp.int32)) // SPAN
    picker = (video_of[:, None] == jnp.arange(VIDS, dtype=jnp.int32)[None, :]).astype(jnp.float32)
    gains = jnp.dot(picker, gate[0], precision=lax.Precision.HIGHEST)
    width = out_proj.shape[2]
    pieces = 4
    step = width // pieces
    outs = []
    for c in range(pieces):
        cols = slice(c * step, (c + 1) * step)
        partial = jnp.dot(heads_all, out_proj[0, :, cols], preferred_element_type=jnp.float32)
        shares = partial.astype(jnp.bfloat16).reshape(devices, own_rows, step)
        shares = lax.all_to_all(shares, "sp", 0, 0, tiled=True)
        projected = jnp.sum(shares.astype(jnp.float32), axis=0)
        layer_out = resid[0, :, cols] + gains[:, cols] * projected
        outs.append(passed_along(layer_out, "section", 1))
    return jnp.concatenate(outs, axis=1)[None]


def solution(mesh):
    in_specs = (
        P("section", "sp", None),
        P("section", "sp", None, None),
        P("section", None, None, None, "sp"),
        P("section", "sp", None),
        P("section", None, None),
        P("section"),
        P("section"),
        P(),
    )
    out_specs = P("section", "sp", None)
    return jax.shard_map(
        per_device, mesh=mesh, in_specs=in_specs, out_specs=out_specs, check_vma=False
    )
```

```python
import jax
import jax.numpy as jnp
from jax import lax
from jax.experimental import pallas as pl
from jax.experimental.pallas import tpu as pltpu
from jax.sharding import PartitionSpec as P

HDIM = 128
SPAN = 448
NCHUNK = 40
SLOTS = 3
VIDS = 2
TOKS = 896
KEYS = 1344


def passed_along(shard, axis, by):
    devices = lax.axis_size(axis)
    return lax.ppermute(shard, axis, [(i, (i + by) % devices) for i in range(devices)])


def visible_slots(span_id, filled, span_mask):
    row_mask = lax.dynamic_index_in_dim(span_mask, span_id, 0, keepdims=False)
    slot_ids = jnp.arange(SLOTS, dtype=jnp.int32)
    wanted = span_id - 1 - slot_ids
    columns = jnp.arange(NCHUNK, dtype=jnp.int32)
    looked = jnp.sum(jnp.where(columns[None, :] == wanted[:, None], row_mask[None, :], 0), axis=1)
    return (slot_ids < filled) & (looked == 1)


def attend_kernel(bias_ref, own_ref, kc_ref, vc_ref, out_ref):
    score_scale = HDIM ** (-0.5)
    local_heads = out_ref.shape[1] // HDIM
    width = local_heads * HDIM
    contract = (((1,), (1,)), ((), ()))
    bias = bias_ref[...]
    for h in range(local_heads):
        cols = slice(h * HDIM, (h + 1) * HDIM)
        q = own_ref[:, :, h * HDIM:(h + 1) * HDIM].reshape(SPAN, HDIM)
        kn = own_ref[:, :, width + h * HDIM:width + (h + 1) * HDIM].reshape(SPAN, HDIM)
        vn = own_ref[:, :, 2 * width + h * HDIM:2 * width + (h + 1) * HDIM].reshape(SPAN, HDIM)
        kc = kc_ref[0, 0, :, cols]
        vc = vc_ref[0, 0, :, cols]
        far = lax.dot_general(q, kc, contract, preferred_element_type=jnp.float32) * score_scale
        far = far + bias
        near = lax.dot_general(q, kn, contract, preferred_element_type=jnp.float32) * score_scale
        highest = jnp.maximum(jnp.max(far, axis=1, keepdims=True), jnp.max(near, axis=1, keepdims=True))
        far_raised = jnp.exp(far - highest)
        near_raised = jnp.exp(near - highest)
        total = jnp.sum(far_raised, axis=1, keepdims=True) + jnp.sum(near_raised, axis=1, keepdims=True)
        far_w = (far_raised / total).astype(jnp.bfloat16)
        near_w = (near_raised / total).astype(jnp.bfloat16)
        mixed = jnp.dot(far_w, vc, preferred_element_type=jnp.float32) + jnp.dot(
            near_w, vn, preferred_element_type=jnp.float32
        )
        out_ref[:, cols] = mixed.astype(out_ref.dtype)


def attend_all(key_bias, spread, cache_kv, local_heads):
    groups = spread.shape[0]
    per_video = groups // VIDS
    rows = spread.shape[1]
    width = local_heads * HDIM

    return pl.pallas_call(
        attend_kernel,
        grid=(VIDS,),
        in_specs=[
            pl.BlockSpec((1, KEYS), lambda b: (0, 0)),
            pl.BlockSpec((per_video, rows, 3 * width), lambda b: (b, 0, 0)),
            pl.BlockSpec((1, 1, KEYS, width), lambda b: (0, b, 0, 0)),
            pl.BlockSpec((1, 1, KEYS, width), lambda b: (1, b, 0, 0)),
        ],
        out_specs=pl.BlockSpec((SPAN, width), lambda b: (b, 0)),
        out_shape=jax.ShapeDtypeStruct((TOKS, width), jnp.bfloat16),
    )(key_bias, spread, cache_kv, cache_kv)


def per_device(resid, qkv, cache_kv, out_proj, gate, span_ids, cache_counts, span_mask):
    own_rows = resid.shape[1]
    local_width = cache_kv.shape[4]
    local_heads = local_width // HDIM
    devices = lax.axis_size("sp")
    filled = cache_counts[0]
    live_slots = visible_slots(span_ids[0], filled, span_mask)
    key_bias = jnp.repeat(jnp.where(live_slots, 0.0, -jnp.inf).astype(jnp.float32), SPAN)[None, :]

    grouped = qkv[0].reshape(own_rows, 3, devices, local_width).transpose(2, 0, 1, 3)
    grouped = grouped.reshape(devices, own_rows, 3 * local_width)
    spread = lax.all_to_all(grouped, "sp", 0, 0, tiled=True)
    heads_all = attend_all(key_bias, spread, cache_kv[0], local_heads)

    device_place = lax.axis_index("sp")
    video_of = (device_place * own_rows + jnp.arange(own_rows, dtype=jnp.int32)) // SPAN
    picker = (video_of[:, None] == jnp.arange(VIDS, dtype=jnp.int32)[None, :]).astype(jnp.float32)
    gains = jnp.dot(picker, gate[0], precision=lax.Precision.HIGHEST)
    width = out_proj.shape[2]
    pieces = 2
    step = width // pieces
    outs = []
    for c in range(pieces):
        cols = slice(c * step, (c + 1) * step)
        partial = jnp.dot(heads_all, out_proj[0, :, cols], preferred_element_type=jnp.float32)
        shares = partial.astype(jnp.bfloat16).reshape(devices, own_rows, step)
        shares = lax.all_to_all(shares, "sp", 0, 0, tiled=True)
        projected = jnp.sum(shares.astype(jnp.float32), axis=0)
        layer_out = resid[0, :, cols] + gains[:, cols] * projected
        outs.append(passed_along(layer_out, "section", 1))
    return jnp.concatenate(outs, axis=1)[None]


def solution(mesh):
    in_specs = (
        P("section", "sp", None),
        P("section", "sp", None, None),
        P("section", None, None, None, "sp"),
        P("section", "sp", None),
        P("section", None, None),
        P("section"),
        P("section"),
        P(),
    )
    out_specs = P("section", "sp", None)
    return jax.shard_map(
        per_device, mesh=mesh, in_specs=in_specs, out_specs=out_specs, check_vma=False
    )
```

```python
import jax
import jax.numpy as jnp
from jax import lax
from jax.experimental import pallas as pl
from jax.experimental.pallas import tpu as pltpu
from jax.sharding import PartitionSpec as P

HDIM = 128
SPAN = 448
NCHUNK = 40
SLOTS = 3
VIDS = 2
TOKS = 896
KEYS = 1344


def passed_along(shard, axis, by):
    devices = lax.axis_size(axis)
    return lax.ppermute(shard, axis, [(i, (i + by) % devices) for i in range(devices)])


def visible_slots(span_id, filled, span_mask):
    row_mask = lax.dynamic_index_in_dim(span_mask, span_id, 0, keepdims=False)
    slot_ids = jnp.arange(SLOTS, dtype=jnp.int32)
    wanted = span_id - 1 - slot_ids
    columns = jnp.arange(NCHUNK, dtype=jnp.int32)
    looked = jnp.sum(jnp.where(columns[None, :] == wanted[:, None], row_mask[None, :], 0), axis=1)
    return (slot_ids < filled) & (looked == 1)


def attend_kernel(bias_ref, own_ref, kc_ref, vc_ref, out_ref):
    score_scale = HDIM ** (-0.5)
    local_heads = out_ref.shape[1] // HDIM
    width = local_heads * HDIM
    contract = (((1,), (1,)), ((), ()))
    bias = bias_ref[...]
    for h in range(local_heads):
        cols = slice(h * HDIM, (h + 1) * HDIM)
        q = own_ref[:, :, h * HDIM:(h + 1) * HDIM].reshape(SPAN, HDIM)
        kn = own_ref[:, :, width + h * HDIM:width + (h + 1) * HDIM].reshape(SPAN, HDIM)
        vn = own_ref[:, :, 2 * width + h * HDIM:2 * width + (h + 1) * HDIM].reshape(SPAN, HDIM)
        kc = kc_ref[0, 0, :, cols]
        vc = vc_ref[0, 0, :, cols]
        far = lax.dot_general(q, kc, contract, preferred_element_type=jnp.float32) * score_scale
        far = far + bias
        near = lax.dot_general(q, kn, contract, preferred_element_type=jnp.float32) * score_scale
        highest = jnp.maximum(jnp.max(far, axis=1, keepdims=True), jnp.max(near, axis=1, keepdims=True))
        far_raised = jnp.exp(far - highest)
        near_raised = jnp.exp(near - highest)
        total = jnp.sum(far_raised, axis=1, keepdims=True) + jnp.sum(near_raised, axis=1, keepdims=True)
        inverse = 1.0 / total
        far_w = (far_raised * inverse).astype(jnp.bfloat16)
        near_w = (near_raised * inverse).astype(jnp.bfloat16)
        mixed = jnp.dot(far_w, vc, preferred_element_type=jnp.float32) + jnp.dot(
            near_w, vn, preferred_element_type=jnp.float32
        )
        out_ref[:, cols] = mixed.astype(out_ref.dtype)


def attend_all(key_bias, spread, cache_kv, local_heads):
    groups = spread.shape[0]
    per_video = groups // VIDS
    rows = spread.shape[1]
    width = local_heads * HDIM

    return pl.pallas_call(
        attend_kernel,
        grid=(VIDS,),
        in_specs=[
            pl.BlockSpec((1, KEYS), lambda b: (0, 0)),
            pl.BlockSpec((per_video, rows, 3 * width), lambda b: (b, 0, 0)),
            pl.BlockSpec((1, 1, KEYS, width), lambda b: (0, b, 0, 0)),
            pl.BlockSpec((1, 1, KEYS, width), lambda b: (1, b, 0, 0)),
        ],
        out_specs=pl.BlockSpec((SPAN, width), lambda b: (b, 0)),
        out_shape=jax.ShapeDtypeStruct((TOKS, width), jnp.bfloat16),
    )(key_bias, spread, cache_kv, cache_kv)


def per_device(resid, qkv, cache_kv, out_proj, gate, span_ids, cache_counts, span_mask):
    own_rows = resid.shape[1]
    local_width = cache_kv.shape[4]
    local_heads = local_width // HDIM
    devices = lax.axis_size("sp")
    filled = cache_counts[0]
    live_slots = visible_slots(span_ids[0], filled, span_mask)
    key_bias = jnp.repeat(jnp.where(live_slots, 0.0, -jnp.inf).astype(jnp.float32), SPAN)[None, :]

    grouped = qkv[0].reshape(own_rows, 3, devices, local_width).transpose(2, 0, 1, 3)
    grouped = grouped.reshape(devices, own_rows, 3 * local_width)
    spread = lax.all_to_all(grouped, "sp", 0, 0, tiled=True)
    heads_all = attend_all(key_bias, spread, cache_kv[0], local_heads)

    device_place = lax.axis_index("sp")
    video_of = (device_place * own_rows + jnp.arange(own_rows, dtype=jnp.int32)) // SPAN
    picker = (video_of[:, None] == jnp.arange(VIDS, dtype=jnp.int32)[None, :]).astype(jnp.float32)
    gains = jnp.dot(picker, gate[0], precision=lax.Precision.HIGHEST)
    width = out_proj.shape[2]
    pieces = 3
    step = width // pieces
    outs = []
    for c in range(pieces):
        cols = slice(c * step, (c + 1) * step)
        partial = jnp.dot(heads_all, out_proj[0, :, cols], preferred_element_type=jnp.float32)
        shares = partial.astype(jnp.bfloat16).reshape(devices, own_rows, step)
        shares = lax.all_to_all(shares, "sp", 0, 0, tiled=True)
        projected = jnp.sum(shares.astype(jnp.float32), axis=0)
        layer_out = resid[0, :, cols] + gains[:, cols] * projected
        outs.append(passed_along(layer_out, "section", 1))
    return jnp.concatenate(outs, axis=1)[None]


def solution(mesh):
    in_specs = (
        P("section", "sp", None),
        P("section", "sp", None, None),
        P("section", None, None, None, "sp"),
        P("section", "sp", None),
        P("section", None, None),
        P("section"),
        P("section"),
        P(),
    )
    out_specs = P("section", "sp", None)
    return jax.shard_map(
        per_device, mesh=mesh, in_specs=in_specs, out_specs=out_specs, check_vma=False
    )
```

```python
import jax
import jax.numpy as jnp
from jax import lax
from jax.experimental import pallas as pl
from jax.experimental.pallas import tpu as pltpu
from jax.sharding import PartitionSpec as P

HDIM = 128
SPAN = 448
NCHUNK = 40
SLOTS = 3
VIDS = 2
TOKS = 896
KEYS = 1344


def passed_along(shard, axis, by):
    devices = lax.axis_size(axis)
    return lax.ppermute(shard, axis, [(i, (i + by) % devices) for i in range(devices)])


def visible_slots(span_id, filled, span_mask):
    row_mask = lax.dynamic_index_in_dim(span_mask, span_id, 0, keepdims=False)
    slot_ids = jnp.arange(SLOTS, dtype=jnp.int32)
    wanted = span_id - 1 - slot_ids
    columns = jnp.arange(NCHUNK, dtype=jnp.int32)
    looked = jnp.sum(jnp.where(columns[None, :] == wanted[:, None], row_mask[None, :], 0), axis=1)
    return (slot_ids < filled) & (looked == 1)


def attend_kernel(bias_ref, own_ref, kc_ref, vc_ref, out_ref):
    score_scale = HDIM ** (-0.5)
    local_heads = out_ref.shape[1] // HDIM
    width = local_heads * HDIM
    contract = (((1,), (1,)), ((), ()))
    bias = bias_ref[...]
    for h in range(local_heads):
        cols = slice(h * HDIM, (h + 1) * HDIM)
        q = own_ref[:, :, h * HDIM:(h + 1) * HDIM].reshape(SPAN, HDIM)
        kn = own_ref[:, :, width + h * HDIM:width + (h + 1) * HDIM].reshape(SPAN, HDIM)
        vn = own_ref[:, :, 2 * width + h * HDIM:2 * width + (h + 1) * HDIM].reshape(SPAN, HDIM)
        kc = kc_ref[0, 0, :, cols]
        vc = vc_ref[0, 0, :, cols]
        far = lax.dot_general(q, kc, contract, preferred_element_type=jnp.float32) * score_scale
        far = far + bias
        near = lax.dot_general(q, kn, contract, preferred_element_type=jnp.float32) * score_scale
        highest = jnp.maximum(jnp.max(far, axis=1, keepdims=True), jnp.max(near, axis=1, keepdims=True))
        far_raised = jnp.exp(far - highest)
        near_raised = jnp.exp(near - highest)
        total = jnp.sum(far_raised, axis=1, keepdims=True) + jnp.sum(near_raised, axis=1, keepdims=True)
        inverse = 1.0 / total
        far_w = (far_raised * inverse).astype(jnp.bfloat16)
        near_w = (near_raised * inverse).astype(jnp.bfloat16)
        mixed = jnp.dot(far_w, vc, preferred_element_type=jnp.float32) + jnp.dot(
            near_w, vn, preferred_element_type=jnp.float32
        )
        out_ref[:, cols] = mixed.astype(out_ref.dtype)


def attend_all(key_bias, spread, cache_kv, local_heads):
    groups = spread.shape[0]
    per_video = groups // VIDS
    rows = spread.shape[1]
    width = local_heads * HDIM

    return pl.pallas_call(
        attend_kernel,
        grid=(VIDS,),
        in_specs=[
            pl.BlockSpec((1, KEYS), lambda b: (0, 0)),
            pl.BlockSpec((per_video, rows, 3 * width), lambda b: (b, 0, 0)),
            pl.BlockSpec((1, 1, KEYS, width), lambda b: (0, b, 0, 0)),
            pl.BlockSpec((1, 1, KEYS, width), lambda b: (1, b, 0, 0)),
        ],
        out_specs=pl.BlockSpec((SPAN, width), lambda b: (b, 0)),
        out_shape=jax.ShapeDtypeStruct((TOKS, width), jnp.bfloat16),
    )(key_bias, spread, cache_kv, cache_kv)


def per_device(resid, qkv, cache_kv, out_proj, gate, span_ids, cache_counts, span_mask):
    own_rows = resid.shape[1]
    local_width = cache_kv.shape[4]
    local_heads = local_width // HDIM
    devices = lax.axis_size("sp")
    filled = cache_counts[0]
    live_slots = visible_slots(span_ids[0], filled, span_mask)
    key_bias = jnp.repeat(jnp.where(live_slots, 0.0, -jnp.inf).astype(jnp.float32), SPAN)[None, :]

    grouped = qkv[0].reshape(own_rows, 3, devices, local_width).transpose(2, 0, 1, 3)
    grouped = grouped.reshape(devices, own_rows, 3 * local_width)
    spread = lax.all_to_all(grouped, "sp", 0, 0, tiled=True)
    heads_all = attend_all(key_bias, spread, cache_kv[0], local_heads)

    device_place = lax.axis_index("sp")
    video_of = (device_place * own_rows + jnp.arange(own_rows, dtype=jnp.int32)) // SPAN
    picker = (video_of[:, None] == jnp.arange(VIDS, dtype=jnp.int32)[None, :]).astype(jnp.float32)
    gains = jnp.dot(picker, gate[0], precision=lax.Precision.HIGHEST)
    width = out_proj.shape[2]
    unit = width // 12
    bounds = [0, 5 * unit, 9 * unit, width]
    outs = []
    for c in range(len(bounds) - 1):
        cols = slice(bounds[c], bounds[c + 1])
        step = bounds[c + 1] - bounds[c]
        partial = jnp.dot(heads_all, out_proj[0, :, cols], preferred_element_type=jnp.float32)
        shares = partial.astype(jnp.bfloat16).reshape(devices, own_rows, step)
        shares = lax.all_to_all(shares, "sp", 0, 0, tiled=True)
        projected = jnp.sum(shares.astype(jnp.float32), axis=0)
        layer_out = resid[0, :, cols] + gains[:, cols] * projected
        outs.append(passed_along(layer_out, "section", 1))
    return jnp.concatenate(outs, axis=1)[None]


def solution(mesh):
    in_specs = (
        P("section", "sp", None),
        P("section", "sp", None, None),
        P("section", None, None, None, "sp"),
        P("section", "sp", None),
        P("section", None, None),
        P("section"),
        P("section"),
        P(),
    )
    out_specs = P("section", "sp", None)
    return jax.shard_map(
        per_device, mesh=mesh, in_specs=in_specs, out_specs=out_specs, check_vma=False
    )
```
